256 devices in a mesh: seq: 8 (over z), exp: 8 (over x, y_hi), img: 4 (over y_lo, core).
Axes of the slice: x: 4, y: 4 (y_hi: 2, y_lo: 2; y = y_hi * 2 + y_lo), z: 8, core: 2. Of those that a mesh axis runs over, the one named last changes fastest.
Arguments:
- projected: bfloat16 [32, 1024, 3, 1280], P(('img', 'exp'), 'seq'), parts along dimension 0, may hold values from -6 to 6
- residual: bfloat16 [32, 1024, 1280], P(('img', 'exp'), 'seq'), parts along dimension 0, may hold values from -6 to 6
- attn_proj: bfloat16 [1280, 1280], P('seq'), may hold values from -0.15625 to 0.15625
- norm_gain: float32 [1280], replicated, may hold values from 0.5 to 2
- norm_bias: float32 [1280], replicated, may hold values from -3 to 3
- expert_ids: int32 [32, 1024, 1], P(('img', 'exp')), parts along dimension 0, may hold values from 0 to 15; in each aligned block of 128 rows (0 to 127, 128 to 255, ..., all dimensions but the last counted through in order) at most 12 rows name the same one
- expert_up: bfloat16 [16, 1280, 5120], P('exp', None, 'seq'), may hold values from -0.15625 to 0.15625
- expert_down: bfloat16 [16, 5120, 1280], P('exp', 'seq'), may hold values from -0.078125 to 0.078125
Outputs:
- layer_out: bfloat16 [32, 1024, 1280], P(('img', 'exp'), 'seq'), parts along dimension 0
The draws below stay inside these ranges and needn't reach their ends.
There are 4 independent parts, one for each index of `img`. The reference program is written for one: setup_inputs(seed, part) draws one part's arguments, and reference() takes and returns one part's arrays. A program takes and returns all parts, laid end to end along the dimension named above; an argument that names none is the same for every part. Nothing has to cross between parts.
Inputs may be any that keep to these rules, and one draw needn't show every extreme that they name: `expert_ids`: in each sequence, within every aligned block of 128 tokens, no expert is named by more than 12 tokens.
All inputs are finite; a program needn't handle non-finite values.
Results may differ from the reference program's by a relative error of at most 0.015.
Values may be sent and summed in bfloat16 or wider, within the bound.
No kernel may reach another device: no remote copies, remote signals or barrier semaphores. Data moves between devices by JAX's collectives and lax.ppermute only.
A program may use at most 64 MiB of HBM per device.

```python
import math
import jax
import jax.numpy as jnp
import numpy as np
from jax import lax

D = 1280
HEADS = 16
HEAD_DIM = 80
HID = 5120
EXPERTS = 16
TOK_DEV = 128
LENGTH = 1024
SEQS = 8
CAP_DEV = 12
CAP = 96
N_SEQ = 8


def draw_projected(key, part):
    shape = (SEQS, LENGTH, 3, D)
    result = jnp.clip(jax.random.normal(key, shape, jnp.float32), -6.0, 6.0)
    return result.astype(jnp.bfloat16)


def block_scale(stream_key, shape, split, smallest, largest):
    loudness, own = 1.0, jax.random.fold_in(stream_key, 6)
    for position, parts in split:
        steps = jnp.exp(jax.random.uniform(jax.random.fold_in(own, position), (parts,), jnp.float32, smallest / len(split), largest / len(split)))
        loudness = loudness * jnp.repeat(steps, shape[position] // parts).reshape([-1 if axis == position else 1 for axis in range(len(shape))])
    return loudness


def deal_out(key, own, number, rows, count, top, most, lean):
    sequence = jax.random.permutation(key, count)
    heavy_load, common = portions_of(count, rows * top, most, lean, True), portions_of(count, rows * top, most, lean, False)
    places = jnp.arange(count)

    def named(sizes, turn):
        used = int((sizes > 0).sum())
        fixed = max(1, used // 4)
        passed = fixed + (places - fixed + turn * (used - fixed)) % max(1, count - fixed)
        return jnp.zeros((count,), jnp.int32).at[sequence[jnp.where(places < fixed, places, passed)]].set(jnp.asarray(sizes, jnp.int32))

    sizes = jnp.where(number % 4 == 0, named(heavy_load, number // 4), named(common, number - number // 4 - 1))
    mixed = jax.random.permutation(jax.random.fold_in(own, 3), count)
    source_of, receiver = mixed[0:count // 2 * 2:2], mixed[1:count // 2 * 2:2]
    margin = jnp.minimum(sizes[source_of] - 1, most - sizes[receiver]) // 2
    margin = jnp.where((source_of == sequence[0]) | (receiver == sequence[0]) | (sizes[receiver] == 0), 0, jnp.maximum(margin, 0))
    passed = jax.random.randint(jax.random.fold_in(own, 4), (count // 2,), 0, 1 << 20) % (margin + 1)
    sizes = sizes.at[source_of].add(-passed).at[receiver].add(passed)
    labels = jnp.searchsorted(jnp.cumsum(sizes), jnp.arange(rows * top), side="right").astype(jnp.int32)
    table = labels.reshape(top, rows).T
    table = table[jax.random.permutation(jax.random.fold_in(own, 1), rows)]
    turn = jax.random.randint(jax.random.fold_in(own, 2), (rows, 1), 0, top)
    return jnp.take_along_axis(table, (jnp.arange(top)[None, :] + turn) % top, axis=1)


def portions_of(count, total, limit, slope, full):
    portions = [(1 << 20) // math.isqrt(grade ** slope) + 1 for grade in range(1, count + 1)]
    largest = limit if full else min(limit, max(-(-total // count), total * portions[0] // sum(portions)))
    least = 1 if total - largest >= count - 1 else 0
    counts, spare = [largest] + [least] * (count - 1), total - largest - least * (count - 1)
    while spare > 0:
        free = [i for i in range(1, count) if counts[i] < largest] or [i for i in range(1, count) if counts[i] < limit]
        pool, left = sum([portions[i] for i in free]), spare
        for i in free:
            extra = min(limit - counts[i], max(1, left * portions[i] // pool), spare)
            counts[i] = counts[i] + extra
            spare = spare - extra
    return np.array(counts)


def gaussian(rng, shape, scale, bound, cuts=(), held_as=jnp.bfloat16):
    drawn = jax.random.normal(rng, shape, jnp.float32) * scale
    if len(cuts) > 0:
        drawn = block_scale(rng, shape, cuts, -0.22, 0.18) * drawn
    return jnp.clip(drawn, min=-bound, max=bound).astype(held_as)


def setup_inputs(seed: int = 0, part: int = 0) -> dict:
    streams_of = jax.random.split(jax.random.key(seed), 9)
    own_keys = jax.random.split(jax.random.fold_in(streams_of[8], part), 9)
    projected = draw_projected(jax.random.fold_in(jax.random.fold_in(streams_of[8], part), 71), part)
    residual = gaussian(own_keys[1], (SEQS, LENGTH, D), 1.0, 6.0, ((0, 8), (1, 8)))
    attn_proj = gaussian(streams_of[2], (D, D), D ** -0.5, 0.15625, ((0, 8),))
    norm_gain = jnp.clip(jnp.exp(jax.random.uniform(streams_of[3], (D,), jnp.float32, math.log(0.5), math.log(2.0))), 0.5, 2.0)
    norm_bias = gaussian(streams_of[4], (D,), 0.5, 3.0, (), jnp.float32)
    expert_ids_keys = jax.random.split(jax.random.fold_in(own_keys[5], 1), SEQS * LENGTH // TOK_DEV)
    expert_ids_turns = jax.random.permutation(jax.random.fold_in(own_keys[5], 3), SEQS * LENGTH // TOK_DEV)
    expert_ids = jax.vmap(lambda own, number: deal_out(jax.random.fold_in(own_keys[5], 2), own, number, TOK_DEV, EXPERTS, 1, CAP_DEV, 1))(expert_ids_keys, expert_ids_turns).reshape((SEQS, LENGTH, 1))
    expert_up = gaussian(streams_of[6], (EXPERTS, D, HID), D ** -0.5, 0.15625, ((0, 8), (2, 8)))
    expert_down = gaussian(streams_of[7], (EXPERTS, HID, D), HID ** -0.5, 0.078125, ((0, 8), (1, 8)))
    return dict(projected=projected, residual=residual, attn_proj=attn_proj, norm_gain=norm_gain, norm_bias=norm_bias, expert_ids=expert_ids, expert_up=expert_up, expert_down=expert_down)


def attention(proj_seq):
    length = proj_seq.shape[0]
    grouped = proj_seq.reshape(length, 3, HEADS, HEAD_DIM)
    queries = grouped[:, 0]
    keys_all = grouped[:, 1].astype(jnp.float32)
    values = grouped[:, 2].astype(jnp.float32)
    span_rows = min(512, length)
    factor = 1.0 / HEAD_DIM ** 0.5

    def one_block(offset):
        query_rows = lax.dynamic_slice_in_dim(queries, offset, span_rows, 0).astype(jnp.float32)
        scores = jnp.einsum('qhd,khd->hqk', query_rows, keys_all) * factor
        peak = lax.optimization_barrier(jnp.max(scores, axis=-1, keepdims=True))
        powers = jnp.exp(scores - peak)
        weights = (powers / lax.optimization_barrier(jnp.sum(powers, axis=-1, keepdims=True))).astype(jnp.bfloat16)
        mixed = jnp.einsum('hqk,khd->qhd', weights.astype(jnp.float32), values)
        return mixed.astype(jnp.bfloat16)
    starts = jnp.arange(length // span_rows, dtype=jnp.int32) * span_rows
    blocks = lax.map(one_block, starts)
    return blocks.reshape(length, HEADS * HEAD_DIM)

def layer_norm(stream, norm_gain, norm_bias):
    values = stream.astype(jnp.float32)
    centre = lax.optimization_barrier(jnp.mean(values, axis=-1, keepdims=True))
    centered = values - centre
    variance = lax.optimization_barrier(jnp.mean(centered * centered, axis=-1, keepdims=True))
    return (centered / jnp.sqrt(variance + 1e-06) * norm_gain + norm_bias).astype(jnp.bfloat16)

def slot_numbers(ids_flat, tok_rows, experts, cap_dev, block_count):
    length = ids_flat.shape[0]
    onehot = (ids_flat[:, None] == jnp.arange(experts, dtype=jnp.int32)[None, :]).astype(jnp.int32)
    blocks = onehot.reshape(block_count, tok_rows, experts)
    before = jnp.cumsum(blocks, axis=1) - blocks
    order_in_block = lax.optimization_barrier(jnp.sum(before * blocks, axis=2)).reshape(length)
    block_id = jnp.arange(length, dtype=jnp.int32) // tok_rows
    slot_all = ids_flat * (cap_dev * block_count) + block_id * cap_dev + order_in_block
    return slot_all.astype(jnp.int32)

def reference(projected, residual, attn_proj, norm_gain, norm_bias, expert_ids, expert_up, expert_down):
    width = HID // N_SEQ
    down_split = expert_down.reshape(EXPERTS, N_SEQ, width, D).astype(jnp.float32)
    up_float = expert_up.astype(jnp.float32)

    def one_sequence(inputs):
        proj_seq, resid_seq, ids_seq = inputs
        attended = attention(proj_seq)
        stream = (resid_seq.astype(jnp.float32) + jnp.dot(attended, attn_proj, preferred_element_type=jnp.float32)).astype(jnp.bfloat16)
        normed = layer_norm(stream, norm_gain, norm_bias)
        ids_flat = ids_seq[:, 0].astype(jnp.int32)
        slot_all = slot_numbers(ids_flat, TOK_DEV, EXPERTS, CAP_DEV, N_SEQ)
        buffer = jnp.zeros((EXPERTS * CAP, D), jnp.bfloat16).at[slot_all].set(normed).reshape(EXPERTS, CAP, D)
        hidden = jax.nn.gelu(jnp.einsum('ecd,edf->ecf', buffer.astype(jnp.float32), up_float), approximate=False).astype(jnp.bfloat16)
        hidden_split = hidden.reshape(EXPERTS, CAP, N_SEQ, width).astype(jnp.float32)
        pieces = jnp.einsum('eckf,ekfd->eckd', hidden_split, down_split).astype(jnp.bfloat16)
        summed = lax.optimization_barrier(jnp.sum(pieces.astype(jnp.float32), axis=2)).reshape(EXPERTS * CAP, D)
        expert_out = jnp.take(summed, slot_all, axis=0)
        return (stream.astype(jnp.float32) + expert_out).astype(jnp.bfloat16)
    return lax.map(one_sequence, (projected, residual, expert_ids))
```

```python
import jax
import jax.numpy as jnp
from jax import lax
from jax.sharding import PartitionSpec as P

HEADS = 16
HEAD_DIM = 80


def attend(gathered):
    queries = gathered[:, 0, 0]
    keys_all = gathered[:, 1, 0]
    values = gathered[:, 2, 0]
    length = queries.shape[0]
    span_rows = min(512, length)
    factor = 1.0 / queries.shape[2] ** 0.5

    def one_block(offset):
        query_rows = lax.dynamic_slice_in_dim(queries, offset, span_rows, 0)
        scores = (
            jnp.einsum("qhd,khd->hqk", query_rows, keys_all, preferred_element_type=jnp.float32)
            * factor
        )
        peak = jnp.max(scores, axis=-1, keepdims=True)
        powers = jnp.exp(scores - peak)
        weights = (powers / jnp.sum(powers, axis=-1, keepdims=True)).astype(jnp.bfloat16)
        mixed = jnp.einsum("hqk,khd->qhd", weights, values, preferred_element_type=jnp.float32)
        return mixed.astype(jnp.bfloat16)

    starts = jnp.arange(length // span_rows, dtype=jnp.int32) * span_rows
    blocks = lax.map(one_block, starts)
    return blocks.reshape(length, queries.shape[1], queries.shape[2])


def layer_norm(stream, norm_gain, norm_bias):
    values = stream.astype(jnp.float32)
    centre = jnp.mean(values, axis=-1, keepdims=True)
    centered = values - centre
    variance = jnp.mean(centered * centered, axis=-1, keepdims=True)
    return (centered / jnp.sqrt(variance + 1e-06) * norm_gain + norm_bias).astype(jnp.bfloat16)


def per_device(
    projected, residual, attn_proj, norm_gain, norm_bias, expert_ids, expert_up, expert_down
):
    tok_rows = projected.shape[1]
    model_width = projected.shape[3]
    seq_count = lax.axis_size("seq")
    exp_count = lax.axis_size("exp")
    local_experts = expert_up.shape[0]
    experts = local_experts * exp_count
    cap_dev = 3 * tok_rows // (2 * experts)
    capacity = cap_dev * seq_count
    length = tok_rows * seq_count
    heads_here = HEADS // seq_count
    head_width = heads_here * HEAD_DIM
    regrouped = projected[0].reshape(tok_rows, 3, seq_count, heads_here, HEAD_DIM)
    attended = attend(lax.all_to_all(regrouped, "seq", split_axis=2, concat_axis=0, tiled=True))
    attended = attended.reshape(seq_count, tok_rows, 1, head_width)
    token_heads = lax.all_to_all(attended, "seq", split_axis=0, concat_axis=2, tiled=True).reshape(
        tok_rows, model_width
    )
    projected_sum = jnp.dot(
        token_heads,
        lax.all_gather(attn_proj, "seq", axis=0, tiled=True),
        preferred_element_type=jnp.float32,
    )
    stream_own = residual[0].astype(jnp.float32) + projected_sum
    stream = stream_own.astype(jnp.bfloat16)
    stream_own = stream.astype(jnp.float32)
    normed = layer_norm(stream, norm_gain, norm_bias)
    seq_index = lax.axis_index("seq")
    ids_own = lax.dynamic_slice_in_dim(expert_ids[0, :, 0], seq_index * tok_rows, tok_rows)
    onehot = (ids_own[:, None] == jnp.arange(experts, dtype=jnp.int32)[None, :]).astype(jnp.int32)
    before = jnp.cumsum(onehot, axis=0) - onehot
    order_in_block = jnp.sum(before * onehot, axis=1)
    dest = ids_own * cap_dev + order_in_block
    select = (dest[:, None] == jnp.arange(experts * cap_dev, dtype=jnp.int32)[None, :]).astype(
        jnp.bfloat16
    )
    dispatch = jnp.einsum(
        "tk,td->kd", select, normed, preferred_element_type=jnp.float32
    ).astype(jnp.bfloat16)
    dispatch = dispatch.reshape(exp_count, local_experts, cap_dev, model_width)
    arrived = lax.all_to_all(dispatch, "exp", split_axis=0, concat_axis=0, tiled=True)
    gathered = lax.all_gather(arrived, "seq", axis=0, tiled=False)
    hidden = jax.nn.gelu(
        jnp.einsum("sejcd,jdf->sejcf", gathered, expert_up, preferred_element_type=jnp.float32),
        approximate=False,
    ).astype(jnp.bfloat16)
    pieces = jnp.einsum(
        "sejcf,jfd->sejcd", hidden, expert_down, preferred_element_type=jnp.float32
    ).astype(jnp.bfloat16)
    summed = lax.psum_scatter(pieces, "seq", scatter_dimension=0, tiled=True)[0]
    returned = lax.all_to_all(summed, "exp", split_axis=0, concat_axis=0, tiled=True).reshape(
        experts * cap_dev, model_width
    )
    expert_out = jnp.einsum("tk,kd->td", select, returned, preferred_element_type=jnp.float32)
    return (stream_own + expert_out).astype(jnp.bfloat16)[None]


def solution(mesh):
    return jax.shard_map(
        per_device,
        mesh=mesh,
        in_specs=(
            P(("img", "exp"), "seq", None, None),
            P(("img", "exp"), "seq", None),
            P("seq", None),
            P(),
            P(),
            P(("img", "exp"), None, None),
            P("exp", None, "seq"),
            P("exp", "seq", None),
        ),
        out_specs=P(("img", "exp"), "seq", None),
        check_vma=False,
    )
```

```python
import jax
import jax.numpy as jnp
from jax import lax
from jax.sharding import PartitionSpec as P

HEADS = 16
HEAD_DIM = 80


def attend(gathered):
    queries = gathered[:, 0, 0]
    keys_all = gathered[:, 1, 0]
    values = gathered[:, 2, 0]
    length = queries.shape[0]
    span_rows = min(512, length)
    factor = 1.0 / queries.shape[2] ** 0.5

    def one_block(offset):
        query_rows = lax.dynamic_slice_in_dim(queries, offset, span_rows, 0)
        scores = (
            jnp.einsum("qhd,khd->hqk", query_rows, keys_all, preferred_element_type=jnp.float32)
            * factor
        )
        peak = jnp.max(scores, axis=-1, keepdims=True)
        powers = jnp.exp(scores - peak)
        weights = (powers / jnp.sum(powers, axis=-1, keepdims=True)).astype(jnp.bfloat16)
        mixed = jnp.einsum("hqk,khd->qhd", weights, values, preferred_element_type=jnp.float32)
        return mixed.astype(jnp.bfloat16)

    starts = jnp.arange(length // span_rows, dtype=jnp.int32) * span_rows
    blocks = lax.map(one_block, starts)
    return blocks.reshape(length, queries.shape[1], queries.shape[2])


def layer_norm(stream, norm_gain, norm_bias):
    values = stream.astype(jnp.float32)
    centre = jnp.mean(values, axis=-1, keepdims=True)
    centered = values - centre
    variance = jnp.mean(centered * centered, axis=-1, keepdims=True)
    return (centered / jnp.sqrt(variance + 1e-06) * norm_gain + norm_bias).astype(jnp.bfloat16)


def per_device(
    projected, residual, attn_proj, norm_gain, norm_bias, expert_ids, expert_up, expert_down
):
    tok_rows = projected.shape[1]
    model_width = projected.shape[3]
    seq_count = lax.axis_size("seq")
    exp_count = lax.axis_size("exp")
    local_experts = expert_up.shape[0]
    experts = local_experts * exp_count
    cap_dev = 3 * tok_rows // (2 * experts)
    capacity = cap_dev * seq_count
    length = tok_rows * seq_count
    heads_here = HEADS // seq_count
    head_width = heads_here * HEAD_DIM
    regrouped = projected[0].reshape(tok_rows, 3, seq_count, heads_here, HEAD_DIM)
    attended = attend(lax.all_to_all(regrouped, "seq", split_axis=2, concat_axis=0, tiled=True))
    attended = attended.reshape(seq_count, tok_rows, 1, head_width)
    token_heads = lax.all_to_all(attended, "seq", split_axis=0, concat_axis=2, tiled=True).reshape(
        tok_rows, model_width
    )
    projected_sum = jnp.dot(
        token_heads,
        lax.all_gather(attn_proj, "seq", axis=0, tiled=True),
        preferred_element_type=jnp.float32,
    )
    stream_own = residual[0].astype(jnp.float32) + projected_sum
    stream = stream_own.astype(jnp.bfloat16)
    stream_own = stream.astype(jnp.float32)
    normed = layer_norm(stream, norm_gain, norm_bias)
    seq_index = lax.axis_index("seq")
    ids_own = lax.dynamic_slice_in_dim(expert_ids[0, :, 0], seq_index * tok_rows, tok_rows)
    onehot = (ids_own[:, None] == jnp.arange(experts, dtype=jnp.int32)[None, :]).astype(jnp.int32)
    before = jnp.cumsum(onehot, axis=0) - onehot
    order_in_block = jnp.sum(before * onehot, axis=1)
    dest = (ids_own // local_experts) * cap_dev + order_in_block
    columns = jnp.arange(exp_count * cap_dev, dtype=jnp.int32)[None, :]
    expert_out = stream_own
    for local in range(local_experts):
        select = (
            (dest[:, None] == columns) & (ids_own % local_experts == local)[:, None]
        ).astype(jnp.bfloat16)
        dispatch = jnp.einsum(
            "tk,td->kd", select, normed, preferred_element_type=jnp.float32
        ).astype(jnp.bfloat16)
        arrived = lax.all_to_all(
            dispatch.reshape(exp_count, cap_dev, model_width),
            "exp",
            split_axis=0,
            concat_axis=0,
            tiled=True,
        )
        gathered = lax.all_gather(arrived, "seq", axis=0, tiled=True).reshape(-1, model_width)
        hidden = jax.nn.gelu(
            jnp.dot(gathered, expert_up[local], preferred_element_type=jnp.float32),
            approximate=False,
        ).astype(jnp.bfloat16)
        pieces = jnp.dot(hidden, expert_down[local], preferred_element_type=jnp.float32).astype(
            jnp.bfloat16
        )
        summed = lax.psum_scatter(
            pieces.reshape(-1, cap_dev, model_width), "seq", scatter_dimension=0, tiled=True
        )
        returned = lax.all_to_all(
            summed, "exp", split_axis=0, concat_axis=0, tiled=True
        ).reshape(exp_count * cap_dev, model_width)
        expert_out = expert_out + jnp.einsum(
            "tk,kd->td", select, returned, preferred_element_type=jnp.float32
        )
    return expert_out.astype(jnp.bfloat16)[None]


def solution(mesh):
    return jax.shard_map(
        per_device,
        mesh=mesh,
        in_specs=(
            P(("img", "exp"), "seq", None, None),
            P(("img", "exp"), "seq", None),
            P("seq", None),
            P(),
            P(),
            P(("img", "exp"), None, None),
            P("exp", None, "seq"),
            P("exp", "seq", None),
        ),
        out_specs=P(("img", "exp"), "seq", None),
        check_vma=False,
    )
```

```python
import jax
import jax.numpy as jnp
from jax import lax
from jax.sharding import PartitionSpec as P

HEADS = 16
HEAD_DIM = 80


def attend(gathered):
    queries = gathered[:, 0, 0]
    keys_all = gathered[:, 1, 0]
    values = gathered[:, 2, 0]
    length = queries.shape[0]
    span_rows = min(512, length)
    factor = 1.0 / queries.shape[2] ** 0.5

    def one_block(offset):
        query_rows = lax.dynamic_slice_in_dim(queries, offset, span_rows, 0)
        scores = (
            jnp.einsum("qhd,khd->hqk", query_rows, keys_all, preferred_element_type=jnp.float32)
            * factor
        )
        peak = jnp.max(scores, axis=-1, keepdims=True)
        powers = jnp.exp(scores - peak)
        weights = (powers / jnp.sum(powers, axis=-1, keepdims=True)).astype(jnp.bfloat16)
        mixed = jnp.einsum("hqk,khd->qhd", weights, values, preferred_element_type=jnp.float32)
        return mixed.astype(jnp.bfloat16)

    starts = jnp.arange(length // span_rows, dtype=jnp.int32) * span_rows
    blocks = lax.map(one_block, starts)
    return blocks.reshape(length, queries.shape[1], queries.shape[2])


def layer_norm(stream, norm_gain, norm_bias):
    values = stream.astype(jnp.float32)
    centre = jnp.mean(values, axis=-1, keepdims=True)
    centered = values - centre
    variance = jnp.mean(centered * centered, axis=-1, keepdims=True)
    return (centered / jnp.sqrt(variance + 1e-06) * norm_gain + norm_bias).astype(jnp.bfloat16)


def per_device(
    projected, residual, attn_proj, norm_gain, norm_bias, expert_ids, expert_up, expert_down
):
    tok_rows = projected.shape[1]
    model_width = projected.shape[3]
    seq_count = lax.axis_size("seq")
    exp_count = lax.axis_size("exp")
    local_experts = expert_up.shape[0]
    experts = local_experts * exp_count
    cap_dev = 3 * tok_rows // (2 * experts)
    capacity = cap_dev * seq_count
    length = tok_rows * seq_count
    heads_here = HEADS // seq_count
    head_width = heads_here * HEAD_DIM
    regrouped = projected[0].reshape(tok_rows, 3, seq_count, heads_here, HEAD_DIM)
    attended = attend(lax.all_to_all(regrouped, "seq", split_axis=2, concat_axis=0, tiled=True))
    attended = attended.reshape(seq_count, tok_rows, 1, head_width)
    token_heads = lax.all_to_all(attended, "seq", split_axis=0, concat_axis=2, tiled=True).reshape(
        tok_rows, model_width
    )
    img_count = lax.axis_size("img")
    core = lax.axis_index("img") % 2
    half_width = model_width // 2
    proj_half = lax.all_gather(
        lax.dynamic_slice_in_dim(attn_proj, core * half_width, half_width, axis=1),
        "seq",
        axis=0,
        tiled=True,
    )
    sibling = [(i, i ^ 1) for i in range(img_count)]
    proj_other = lax.ppermute(proj_half, "img", sibling)
    proj_full = jnp.zeros((model_width, model_width), jnp.bfloat16)
    proj_full = lax.dynamic_update_slice_in_dim(proj_full, proj_half, core * half_width, axis=1)
    proj_full = lax.dynamic_update_slice_in_dim(
        proj_full, proj_other, (1 - core) * half_width, axis=1
    )
    projected_sum = jnp.dot(token_heads, proj_full, preferred_element_type=jnp.float32)
    stream_own = residual[0].astype(jnp.float32) + projected_sum
    stream = stream_own.astype(jnp.bfloat16)
    stream_own = stream.astype(jnp.float32)
    normed = layer_norm(stream, norm_gain, norm_bias)
    seq_index = lax.axis_index("seq")
    ids_own = lax.dynamic_slice_in_dim(expert_ids[0, :, 0], seq_index * tok_rows, tok_rows)
    onehot = (ids_own[:, None] == jnp.arange(experts, dtype=jnp.int32)[None, :]).astype(jnp.int32)
    before = jnp.cumsum(onehot, axis=0) - onehot
    order_in_block = jnp.sum(before * onehot, axis=1)
    dest = ids_own * cap_dev + order_in_block
    select = (dest[:, None] == jnp.arange(experts * cap_dev, dtype=jnp.int32)[None, :]).astype(
        jnp.bfloat16
    )
    dispatch = jnp.einsum(
        "tk,td->kd", select, normed, preferred_element_type=jnp.float32
    ).astype(jnp.bfloat16)
    dispatch = dispatch.reshape(exp_count, local_experts, cap_dev, model_width)
    arrived = lax.all_to_all(dispatch, "exp", split_axis=0, concat_axis=0, tiled=True)
    gathered = lax.all_gather(arrived, "seq", axis=0, tiled=False)
    hidden = jax.nn.gelu(
        jnp.einsum("sejcd,jdf->sejcf", gathered, expert_up, preferred_element_type=jnp.float32),
        approximate=False,
    ).astype(jnp.bfloat16)
    pieces = jnp.einsum(
        "sejcf,jfd->sejcd", hidden, expert_down, preferred_element_type=jnp.float32
    ).astype(jnp.bfloat16)
    summed = lax.psum_scatter(pieces, "seq", scatter_dimension=0, tiled=True)[0]
    returned = lax.all_to_all(summed, "exp", split_axis=0, concat_axis=0, tiled=True).reshape(
        experts * cap_dev, model_width
    )
    expert_out = jnp.einsum("tk,kd->td", select, returned, preferred_element_type=jnp.float32)
    return (stream_own + expert_out).astype(jnp.bfloat16)[None]


def solution(mesh):
    return jax.shard_map(
        per_device,
        mesh=mesh,
        in_specs=(
            P(("img", "exp"), "seq", None, None),
            P(("img", "exp"), "seq", None),
            P("seq", None),
            P(),
            P(),
            P(("img", "exp"), None, None),
            P("exp", None, "seq"),
            P("exp", "seq", None),
        ),
        out_specs=P(("img", "exp"), "seq", None),
        check_vma=False,
    )
```

```python
import jax
import jax.numpy as jnp
from jax import lax
from jax.sharding import PartitionSpec as P


HEADS = 16
HEAD_DIM = 80


def attend(gathered):
    queries = gathered[:, 0, 0]
    keys_all = gathered[:, 1, 0]
    values = gathered[:, 2, 0]
    length = queries.shape[0]
    span_rows = min(512, length)
    factor = 1.0 / queries.shape[2] ** 0.5

    def one_block(offset):
        query_rows = lax.dynamic_slice_in_dim(queries, offset, span_rows, 0)
        scores = (
            jnp.einsum("qhd,khd->hqk", query_rows, keys_all, preferred_element_type=jnp.float32)
            * factor
        )
        peak = jnp.max(scores, axis=-1, keepdims=True)
        powers = jnp.exp(scores - peak)
        weights = (powers / jnp.sum(powers, axis=-1, keepdims=True)).astype(jnp.bfloat16)
        mixed = jnp.einsum("hqk,khd->qhd", weights, values, preferred_element_type=jnp.float32)
        return mixed.astype(jnp.bfloat16)

    starts = jnp.arange(length // span_rows, dtype=jnp.int32) * span_rows
    blocks = lax.map(one_block, starts)
    return blocks.reshape(length, queries.shape[1], queries.shape[2])


def layer_norm(stream, norm_gain, norm_bias):
    values = stream.astype(jnp.float32)
    centre = jnp.mean(values, axis=-1, keepdims=True)
    centered = values - centre
    variance = jnp.mean(centered * centered, axis=-1, keepdims=True)
    return (centered / jnp.sqrt(variance + 1e-06) * norm_gain + norm_bias).astype(jnp.bfloat16)


def per_device(
    projected, residual, attn_proj, norm_gain, norm_bias, expert_ids, expert_up, expert_down
):
    tok_rows = projected.shape[1]
    model_width = projected.shape[3]
    seq_count = lax.axis_size("seq")
    exp_count = lax.axis_size("exp")
    local_experts = expert_up.shape[0]
    experts = local_experts * exp_count
    cap_dev = 3 * tok_rows // (2 * experts)
    capacity = cap_dev * seq_count
    length = tok_rows * seq_count
    heads_here = HEADS // seq_count
    head_width = heads_here * HEAD_DIM
    regrouped = projected[0].reshape(tok_rows, 3, seq_count, heads_here, HEAD_DIM)
    attended = attend(lax.all_to_all(regrouped, "seq", split_axis=2, concat_axis=0, tiled=True))
    attended = attended.reshape(seq_count, tok_rows, 1, head_width)
    token_heads = lax.all_to_all(attended, "seq", split_axis=0, concat_axis=2, tiled=True).reshape(
        tok_rows, model_width
    )
    projected_sum = jnp.dot(
        token_heads,
        lax.all_gather(attn_proj, "seq", axis=0, tiled=True),
        preferred_element_type=jnp.float32,
    )
    stream_own = residual[0].astype(jnp.float32) + projected_sum
    stream = stream_own.astype(jnp.bfloat16)
    stream_own = stream.astype(jnp.float32)
    normed = layer_norm(stream, norm_gain, norm_bias)
    seq_index = lax.axis_index("seq")
    ids_own = lax.dynamic_slice_in_dim(expert_ids[0, :, 0], seq_index * tok_rows, tok_rows)
    onehot = (ids_own[:, None] == jnp.arange(experts, dtype=jnp.int32)[None, :]).astype(jnp.int32)
    before = jnp.cumsum(onehot, axis=0) - onehot
    order_in_block = jnp.sum(before * onehot, axis=1)
    exp_index = lax.axis_index("exp")
    turn = (ids_own // local_experts - exp_index) % exp_count
    dest = (turn * local_experts + ids_own % local_experts) * cap_dev + order_in_block
    select = (dest[:, None] == jnp.arange(experts * cap_dev, dtype=jnp.int32)[None, :]).astype(
        jnp.bfloat16
    )
    dispatch = jnp.einsum(
        "tk,td->kd", select, normed, preferred_element_type=jnp.float32
    ).astype(jnp.bfloat16)
    dispatch = dispatch.reshape(exp_count, local_experts, cap_dev, model_width)
    arrived = [dispatch[0]]
    for shift in range(1, exp_count):
        forward = [(i, (i + shift) % exp_count) for i in range(exp_count)]
        arrived.append(lax.ppermute(dispatch[shift], "exp", forward))
    arrived = jnp.stack(arrived)
    gathered = lax.all_gather(arrived, "seq", axis=0, tiled=False)
    hidden = jax.nn.gelu(
        jnp.einsum("sejcd,jdf->sejcf", gathered, expert_up, preferred_element_type=jnp.float32),
        approximate=False,
    ).astype(jnp.bfloat16)
    pieces = jnp.einsum(
        "sejcf,jfd->sejcd", hidden, expert_down, preferred_element_type=jnp.float32
    ).astype(jnp.bfloat16)
    summed = lax.psum_scatter(pieces, "seq", scatter_dimension=0, tiled=True)[0]
    returned = [summed[0]]
    for shift in range(1, exp_count):
        backward = [(i, (i - shift) % exp_count) for i in range(exp_count)]
        returned.append(lax.ppermute(summed[shift], "exp", backward))
    returned = jnp.stack(returned).reshape(experts * cap_dev, model_width)
    expert_out = jnp.einsum("tk,kd->td", select, returned, preferred_element_type=jnp.float32)
    return (stream_own + expert_out).astype(jnp.bfloat16)[None]


def solution(mesh):
    return jax.shard_map(
        per_device,
        mesh=mesh,
        in_specs=(
            P(("img", "exp"), "seq", None, None),
            P(("img", "exp"), "seq", None),
            P("seq", None),
            P(),
            P(),
            P(("img", "exp"), None, None),
            P("exp", None, "seq"),
            P("exp", "seq", None),
        ),
        out_specs=P(("img", "exp"), "seq", None),
        check_vma=False,
    )
```

```python
import jax
import jax.numpy as jnp
from jax import lax
from jax.sharding import PartitionSpec as P

HEADS = 16
HEAD_DIM = 80


def attend(gathered):
    queries = gathered[:, 0, 0]
    keys_all = gathered[:, 1, 0]
    values = gathered[:, 2, 0]
    length = queries.shape[0]
    span_rows = length
    factor = 1.0 / queries.shape[2] ** 0.5

    def one_block(offset):
        query_rows = lax.dynamic_slice_in_dim(queries, offset, span_rows, 0)
        scores = (
            jnp.einsum("qhd,khd->hqk", query_rows, keys_all, preferred_element_type=jnp.float32)
            * factor
        )
        peak = jnp.max(scores, axis=-1, keepdims=True)
        powers = jnp.exp(scores - peak)
        weights = (powers / jnp.sum(powers, axis=-1, keepdims=True)).astype(jnp.bfloat16)
        mixed = jnp.einsum("hqk,khd->qhd", weights, values, preferred_element_type=jnp.float32)
        return mixed.astype(jnp.bfloat16)

    starts = jnp.arange(length // span_rows, dtype=jnp.int32) * span_rows
    blocks = lax.map(one_block, starts)
    return blocks.reshape(length, queries.shape[1], queries.shape[2])


def layer_norm(stream, norm_gain, norm_bias):
    values = stream.astype(jnp.float32)
    centre = jnp.mean(values, axis=-1, keepdims=True)
    centered = values - centre
    variance = jnp.mean(centered * centered, axis=-1, keepdims=True)
    return (centered / jnp.sqrt(variance + 1e-06) * norm_gain + norm_bias).astype(jnp.bfloat16)


def per_device(
    projected, residual, attn_proj, norm_gain, norm_bias, expert_ids, expert_up, expert_down
):
    tok_rows = projected.shape[1]
    model_width = projected.shape[3]
    seq_count = lax.axis_size("seq")
    exp_count = lax.axis_size("exp")
    local_experts = expert_up.shape[0]
    experts = local_experts * exp_count
    cap_dev = 3 * tok_rows // (2 * experts)
    capacity = cap_dev * seq_count
    length = tok_rows * seq_count
    heads_here = HEADS // seq_count
    head_width = heads_here * HEAD_DIM
    regrouped = projected[0].reshape(tok_rows, 3, seq_count, heads_here, HEAD_DIM)
    attended = attend(lax.all_to_all(regrouped, "seq", split_axis=2, concat_axis=0, tiled=True))
    attended = attended.reshape(seq_count, tok_rows, 1, head_width)
    token_heads = lax.all_to_all(attended, "seq", split_axis=0, concat_axis=2, tiled=True).reshape(
        tok_rows, model_width
    )
    projected_sum = jnp.dot(
        token_heads,
        lax.all_gather(attn_proj, "seq", axis=0, tiled=True),
        preferred_element_type=jnp.float32,
    )
    stream_own = residual[0].astype(jnp.float32) + projected_sum
    stream = stream_own.astype(jnp.bfloat16)
    stream_own = stream.astype(jnp.float32)
    normed = layer_norm(stream, norm_gain, norm_bias)
    seq_index = lax.axis_index("seq")
    ids_own = lax.dynamic_slice_in_dim(expert_ids[0, :, 0], seq_index * tok_rows, tok_rows)
    onehot = (ids_own[:, None] == jnp.arange(experts, dtype=jnp.int32)[None, :]).astype(jnp.int32)
    before = jnp.cumsum(onehot, axis=0) - onehot
    order_in_block = jnp.sum(before * onehot, axis=1)
    dest = ids_own * cap_dev + order_in_block
    select = (dest[:, None] == jnp.arange(experts * cap_dev, dtype=jnp.int32)[None, :]).astype(
        jnp.bfloat16
    )
    dispatch = jnp.einsum(
        "tk,td->kd", select, normed, preferred_element_type=jnp.float32
    ).astype(jnp.bfloat16)
    dispatch = dispatch.reshape(exp_count, local_experts, cap_dev, model_width)
    arrived = lax.all_to_all(dispatch, "exp", split_axis=0, concat_axis=0, tiled=True)
    gathered = lax.all_gather(arrived, "seq", axis=0, tiled=False)
    hidden = jax.nn.gelu(
        jnp.einsum("sejcd,jdf->sejcf", gathered, expert_up, preferred_element_type=jnp.float32),
        approximate=False,
    ).astype(jnp.bfloat16)
    pieces = jnp.einsum(
        "sejcf,jfd->sejcd", hidden, expert_down, preferred_element_type=jnp.float32
    ).astype(jnp.bfloat16)
    summed = lax.psum_scatter(pieces, "seq", scatter_dimension=0, tiled=True)[0]
    returned = lax.all_to_all(summed, "exp", split_axis=0, concat_axis=0, tiled=True).reshape(
        experts * cap_dev, model_width
    )
    expert_out = jnp.einsum("tk,kd->td", select, returned, preferred_element_type=jnp.float32)
    return (stream_own + expert_out).astype(jnp.bfloat16)[None]


def solution(mesh):
    return jax.shard_map(
        per_device,
        mesh=mesh,
        in_specs=(
            P(("img", "exp"), "seq", None, None),
            P(("img", "exp"), "seq", None),
            P("seq", None),
            P(),
            P(),
            P(("img", "exp"), None, None),
            P("exp", None, "seq"),
            P("exp", "seq", None),
        ),
        out_specs=P(("img", "exp"), "seq", None),
        check_vma=False,
    )
```

```python
import jax
import jax.numpy as jnp
from jax import lax
from jax.sharding import PartitionSpec as P

HEADS = 16
HEAD_DIM = 80


def attend(gathered):
    queries = gathered[0]
    keys_all = gathered[1]
    values = gathered[2]
    factor = 1.0 / queries.shape[2] ** 0.5
    scores = (
        jnp.einsum("ahdb,chde->habce", queries, keys_all, preferred_element_type=jnp.float32)
        * factor
    )
    peak = jnp.max(scores, axis=(3, 4), keepdims=True)
    powers = jnp.exp(scores - peak)
    weights = (powers / jnp.sum(powers, axis=(3, 4), keepdims=True)).astype(jnp.bfloat16)
    mixed = jnp.einsum("habce,chde->abhd", weights, values, preferred_element_type=jnp.float32)
    return mixed.astype(jnp.bfloat16)


def layer_norm(stream, norm_gain, norm_bias):
    values = stream.astype(jnp.float32)
    centre = jnp.mean(values, axis=-1, keepdims=True)
    centered = values - centre
    variance = jnp.mean(centered * centered, axis=-1, keepdims=True)
    return (centered / jnp.sqrt(variance + 1e-06) * norm_gain + norm_bias).astype(jnp.bfloat16)


def per_device(
    projected, residual, attn_proj, norm_gain, norm_bias, expert_ids, expert_up, expert_down
):
    tok_rows = projected.shape[1]
    model_width = projected.shape[3]
    seq_count = lax.axis_size("seq")
    exp_count = lax.axis_size("exp")
    local_experts = expert_up.shape[0]
    experts = local_experts * exp_count
    cap_dev = 3 * tok_rows // (2 * experts)
    capacity = cap_dev * seq_count
    length = tok_rows * seq_count
    heads_here = HEADS // seq_count
    head_width = heads_here * HEAD_DIM
    token_minor = jnp.transpose(projected[0], (1, 2, 0)).reshape(
        3, seq_count, head_width, tok_rows
    )
    arrived_heads = lax.all_to_all(token_minor, "seq", split_axis=1, concat_axis=1, tiled=True)
    attended = attend(arrived_heads.reshape(3, seq_count, heads_here, HEAD_DIM, tok_rows))
    attended = attended.reshape(seq_count, tok_rows, 1, head_width)
    token_heads = lax.all_to_all(attended, "seq", split_axis=0, concat_axis=2, tiled=True).reshape(
        tok_rows, model_width
    )
    projected_sum = jnp.dot(
        token_heads,
        lax.all_gather(attn_proj, "seq", axis=0, tiled=True),
        preferred_element_type=jnp.float32,
    )
    stream_own = residual[0].astype(jnp.float32) + projected_sum
    stream = stream_own.astype(jnp.bfloat16)
    stream_own = stream.astype(jnp.float32)
    normed = layer_norm(stream, norm_gain, norm_bias)
    seq_index = lax.axis_index("seq")
    ids_own = lax.dynamic_slice_in_dim(expert_ids[0, :, 0], seq_index * tok_rows, tok_rows)
    onehot = (ids_own[:, None] == jnp.arange(experts, dtype=jnp.int32)[None, :]).astype(jnp.int32)
    before = jnp.cumsum(onehot, axis=0) - onehot
    order_in_block = jnp.sum(before * onehot, axis=1)
    dest = ids_own * cap_dev + order_in_block
    select = (dest[:, None] == jnp.arange(experts * cap_dev, dtype=jnp.int32)[None, :]).astype(
        jnp.bfloat16
    )
    dispatch = jnp.einsum(
        "tk,td->kd", select, normed, preferred_element_type=jnp.float32
    ).astype(jnp.bfloat16)
    dispatch = dispatch.reshape(exp_count, local_experts, cap_dev, model_width)
    arrived = lax.all_to_all(dispatch, "exp", split_axis=0, concat_axis=0, tiled=True)
    gathered = lax.all_gather(arrived, "seq", axis=0, tiled=False)
    hidden = jax.nn.gelu(
        jnp.einsum("sejcd,jdf->sejcf", gathered, expert_up, preferred_element_type=jnp.float32),
        approximate=False,
    ).astype(jnp.bfloat16)
    pieces = jnp.einsum(
        "sejcf,jfd->sejcd", hidden, expert_down, preferred_element_type=jnp.float32
    ).astype(jnp.bfloat16)
    summed = lax.psum_scatter(pieces, "seq", scatter_dimension=0, tiled=True)[0]
    returned = lax.all_to_all(summed, "exp", split_axis=0, concat_axis=0, tiled=True).reshape(
        experts * cap_dev, model_width
    )
    expert_out = jnp.einsum("tk,kd->td", select, returned, preferred_element_type=jnp.float32)
    return (stream_own + expert_out).astype(jnp.bfloat16)[None]


def solution(mesh):
    return jax.shard_map(
        per_device,
        mesh=mesh,
        in_specs=(
            P(("img", "exp"), "seq", None, None),
            P(("img", "exp"), "seq", None),
            P("seq", None),
            P(),
            P(),
            P(("img", "exp"), None, None),
            P("exp", None, "seq"),
            P("exp", "seq", None),
        ),
        out_specs=P(("img", "exp"), "seq", None),
        check_vma=False,
    )
```

```python
import jax
import jax.numpy as jnp
from jax import lax
from jax.sharding import PartitionSpec as P

HEADS = 16
HEAD_DIM = 80


def attend(gathered):
    queries = gathered[0]
    keys_all = gathered[1]
    values = gathered[2]
    factor = 1.0 / queries.shape[2] ** 0.5
    scores = (
        jnp.einsum("ahdb,chde->habce", queries, keys_all, preferred_element_type=jnp.float32)
        * factor
    )
    peak = jnp.max(scores, axis=(3, 4), keepdims=True)
    powers = jnp.exp(scores - peak)
    weights = (powers / jnp.sum(powers, axis=(3, 4), keepdims=True)).astype(jnp.bfloat16)
    mixed = jnp.einsum("habce,chde->abhd", weights, values, preferred_element_type=jnp.float32)
    return mixed.astype(jnp.bfloat16)


def layer_norm(stream, norm_gain, norm_bias):
    values = stream.astype(jnp.float32)
    centre = jnp.mean(values, axis=-1, keepdims=True)
    centered = values - centre
    variance = jnp.mean(centered * centered, axis=-1, keepdims=True)
    return (centered / jnp.sqrt(variance + 1e-06) * norm_gain + norm_bias).astype(jnp.bfloat16)


def per_device(
    projected, residual, attn_proj, norm_gain, norm_bias, expert_ids, expert_up, expert_down
):
    tok_rows = projected.shape[1]
    model_width = projected.shape[3]
    seq_count = lax.axis_size("seq")
    exp_count = lax.axis_size("exp")
    local_experts = expert_up.shape[0]
    experts = local_experts * exp_count
    cap_dev = 3 * tok_rows // (2 * experts)
    capacity = cap_dev * seq_count
    length = tok_rows * seq_count
    heads_here = HEADS // seq_count
    head_width = heads_here * HEAD_DIM
    token_minor = jnp.transpose(projected[0], (1, 2, 0)).reshape(
        3, seq_count, head_width, tok_rows
    )
    arrived_heads = lax.all_to_all(token_minor, "seq", split_axis=1, concat_axis=1, tiled=True)
    attended = attend(arrived_heads.reshape(3, seq_count, heads_here, HEAD_DIM, tok_rows))
    attended = attended.reshape(seq_count, tok_rows, 1, head_width)
    token_heads = lax.all_to_all(attended, "seq", split_axis=0, concat_axis=2, tiled=True).reshape(
        tok_rows, model_width
    )
    projected_sum = jnp.dot(
        token_heads,
        lax.all_gather(attn_proj, "seq", axis=0, tiled=True),
        preferred_element_type=jnp.float32,
    )
    stream_own = residual[0].astype(jnp.float32) + projected_sum
    stream = stream_own.astype(jnp.bfloat16)
    stream_own = stream.astype(jnp.float32)
    normed = layer_norm(stream, norm_gain, norm_bias)
    seq_index = lax.axis_index("seq")
    ids_own = lax.dynamic_slice_in_dim(expert_ids[0, :, 0], seq_index * tok_rows, tok_rows)
    onehot = (ids_own[:, None] == jnp.arange(experts, dtype=jnp.int32)[None, :]).astype(jnp.int32)
    before = jnp.cumsum(onehot, axis=0) - onehot
    order_in_block = jnp.sum(before * onehot, axis=1)
    dest = ids_own * cap_dev + order_in_block
    select = (dest[:, None] == jnp.arange(experts * cap_dev, dtype=jnp.int32)[None, :]).astype(
        jnp.bfloat16
    )
    dispatch = jnp.einsum(
        "tk,td->kd", select, normed, preferred_element_type=jnp.float32
    ).astype(jnp.bfloat16)
    dispatch = dispatch.reshape(exp_count, local_experts, cap_dev, model_width)
    arrived = lax.all_to_all(dispatch, "exp", split_axis=0, concat_axis=0, tiled=True)
    gathered = lax.all_gather(arrived, "seq", axis=0, tiled=False)
    pieces = []
    for local in range(local_experts):
        hidden = jax.nn.gelu(
            jnp.einsum(
                "secd,df->secf",
                gathered[:, :, local],
                expert_up[local],
                preferred_element_type=jnp.float32,
            ),
            approximate=False,
        ).astype(jnp.bfloat16)
        piece = jnp.einsum(
            "secf,fd->secd", hidden, expert_down[local], preferred_element_type=jnp.float32
        )
        pieces.append(piece.astype(jnp.bfloat16))
    pieces = jnp.stack(pieces, axis=2)
    summed = lax.psum_scatter(pieces, "seq", scatter_dimension=0, tiled=True)[0]
    returned = lax.all_to_all(summed, "exp", split_axis=0, concat_axis=0, tiled=True).reshape(
        experts * cap_dev, model_width
    )
    expert_out = jnp.einsum("tk,kd->td", select, returned, preferred_element_type=jnp.float32)
    return (stream_own + expert_out).astype(jnp.bfloat16)[None]


def solution(mesh):
    return jax.shard_map(
        per_device,
        mesh=mesh,
        in_specs=(
            P(("img", "exp"), "seq", None, None),
            P(("img", "exp"), "seq", None),
            P("seq", None),
            P(),
            P(),
            P(("img", "exp"), None, None),
            P("exp", None, "seq"),
            P("exp", "seq", None),
        ),
        out_specs=P(("img", "exp"), "seq", None),
        check_vma=False,
    )
```

```python
import jax
import jax.numpy as jnp
from jax import lax
from jax.sharding import PartitionSpec as P

HEADS = 16
HEAD_DIM = 80


def attend(gathered):
    queries = gathered[0]
    keys_all = gathered[1]
    values = gathered[2]
    factor = 1.0 / queries.shape[2] ** 0.5
    scores = (
        jnp.einsum("ahdb,chde->habce", queries, keys_all, preferred_element_type=jnp.float32)
        * factor
    )
    peak = jnp.max(scores, axis=(3, 4), keepdims=True)
    powers = jnp.exp(scores - peak)
    weights = (powers / jnp.sum(powers, axis=(3, 4), keepdims=True)).astype(jnp.bfloat16)
    mixed = jnp.einsum("habce,chde->abhd", weights, values, preferred_element_type=jnp.float32)
    return mixed.astype(jnp.bfloat16)


def layer_norm(stream, norm_gain, norm_bias):
    values = stream.astype(jnp.float32)
    centre = jnp.mean(values, axis=-1, keepdims=True)
    centered = values - centre
    variance = jnp.mean(centered * centered, axis=-1, keepdims=True)
    return (centered / jnp.sqrt(variance + 1e-06) * norm_gain + norm_bias).astype(jnp.bfloat16)


def per_device(
    projected, residual, attn_proj, norm_gain, norm_bias, expert_ids, expert_up, expert_down
):
    tok_rows = projected.shape[1]
    model_width = projected.shape[3]
    seq_count = lax.axis_size("seq")
    exp_count = lax.axis_size("exp")
    local_experts = expert_up.shape[0]
    experts = local_experts * exp_count
    cap_dev = 3 * tok_rows // (2 * experts)
    capacity = cap_dev * seq_count
    length = tok_rows * seq_count
    heads_here = HEADS // seq_count
    head_width = heads_here * HEAD_DIM
    token_minor = jnp.transpose(projected[0], (1, 2, 0)).reshape(
        3, seq_count, head_width, tok_rows
    )
    arrived_heads = lax.all_to_all(token_minor, "seq", split_axis=1, concat_axis=1, tiled=True)
    attended = attend(arrived_heads.reshape(3, seq_count, heads_here, HEAD_DIM, tok_rows))
    attended = attended.reshape(seq_count, tok_rows, 1, head_width)
    token_heads = lax.all_to_all(attended, "seq", split_axis=0, concat_axis=2, tiled=True).reshape(
        tok_rows, model_width
    )
    projected_sum = jnp.dot(
        token_heads,
        lax.all_gather(attn_proj, "seq", axis=0, tiled=True),
        preferred_element_type=jnp.float32,
    )
    stream_own = residual[0].astype(jnp.float32) + projected_sum
    stream = stream_own.astype(jnp.bfloat16)
    stream_own = stream.astype(jnp.float32)
    normed = layer_norm(stream, norm_gain, norm_bias)
    seq_index = lax.axis_index("seq")
    ids_own = lax.dynamic_slice_in_dim(expert_ids[0, :, 0], seq_index * tok_rows, tok_rows)
    onehot = (ids_own[:, None] == jnp.arange(experts, dtype=jnp.int32)[None, :]).astype(jnp.int32)
    before = jnp.cumsum(onehot, axis=0) - onehot
    order_in_block = jnp.sum(before * onehot, axis=1)
    dest = ids_own * cap_dev + order_in_block
    select = (dest[:, None] == jnp.arange(experts * cap_dev, dtype=jnp.int32)[None, :]).astype(
        jnp.bfloat16
    )
    dispatch = jnp.einsum(
        "tk,td->kd", select, normed, preferred_element_type=jnp.float32
    ).astype(jnp.bfloat16)
    dispatch = dispatch.reshape(exp_count, local_experts, cap_dev, model_width)
    arrived = lax.all_to_all(dispatch, "exp", split_axis=0, concat_axis=0, tiled=True)
    gathered = lax.all_gather(arrived, "seq", axis=0, tiled=False)
    pieces = []
    for local in range(local_experts):
        hidden = jax.nn.gelu(
            jnp.einsum(
                "secd,df->secf",
                gathered[:, :, local],
                expert_up[local],
                preferred_element_type=jnp.float32,
            ),
            approximate=False,
        ).astype(jnp.bfloat16)
        hidden = lax.optimization_barrier(hidden)
        piece = jnp.einsum(
            "secf,fd->secd", hidden, expert_down[local], preferred_element_type=jnp.float32
        )
        pieces.append(piece.astype(jnp.bfloat16))
    pieces = jnp.stack(pieces, axis=2)
    summed = lax.psum_scatter(pieces, "seq", scatter_dimension=0, tiled=True)[0]
    returned = lax.all_to_all(summed, "exp", split_axis=0, concat_axis=0, tiled=True).reshape(
        experts * cap_dev, model_width
    )
    expert_out = jnp.einsum("tk,kd->td", select, returned, preferred_element_type=jnp.float32)
    return (stream_own + expert_out).astype(jnp.bfloat16)[None]


def solution(mesh):
    return jax.shard_map(
        per_device,
        mesh=mesh,
        in_specs=(
            P(("img", "exp"), "seq", None, None),
            P(("img", "exp"), "seq", None),
            P("seq", None),
            P(),
            P(),
            P(("img", "exp"), None, None),
            P("exp", None, "seq"),
            P("exp", "seq", None),
        ),
        out_specs=P(("img", "exp"), "seq", None),
        check_vma=False,
    )
```

```python
import jax
import jax.numpy as jnp
from jax import lax
from jax.sharding import PartitionSpec as P

HEADS = 16
HEAD_DIM = 80


def attend(gathered):
    queries = gathered[0]
    keys_all = gathered[1]
    values = gathered[2]
    factor = 1.0 / queries.shape[2] ** 0.5
    scores = (
        jnp.einsum("ahdb,chde->habce", queries, keys_all, preferred_element_type=jnp.float32)
        * factor
    )
    peak = jnp.max(scores, axis=(3, 4), keepdims=True)
    powers = jnp.exp(scores - peak)
    weights = (powers / jnp.sum(powers, axis=(3, 4), keepdims=True)).astype(jnp.bfloat16)
    mixed = jnp.einsum("habce,chde->abhd", weights, values, preferred_element_type=jnp.float32)
    return mixed.astype(jnp.bfloat16)


def layer_norm(stream, norm_gain, norm_bias):
    values = stream.astype(jnp.float32)
    centre = jnp.mean(values, axis=-1, keepdims=True)
    centered = values - centre
    variance = jnp.mean(centered * centered, axis=-1, keepdims=True)
    return (centered / jnp.sqrt(variance + 1e-06) * norm_gain + norm_bias).astype(jnp.bfloat16)


def per_device(
    projected, residual, attn_proj, norm_gain, norm_bias, expert_ids, expert_up, expert_down
):
    tok_rows = projected.shape[1]
    model_width = projected.shape[3]
    seq_count = lax.axis_size("seq")
    exp_count = lax.axis_size("exp")
    local_experts = expert_up.shape[0]
    experts = local_experts * exp_count
    cap_dev = 3 * tok_rows // (2 * experts)
    capacity = cap_dev * seq_count
    length = tok_rows * seq_count
    heads_here = HEADS // seq_count
    head_width = heads_here * HEAD_DIM
    token_minor = jnp.transpose(projected[0], (1, 2, 0)).reshape(
        3, seq_count, head_width, tok_rows
    )
    arrived_heads = lax.all_to_all(token_minor, "seq", split_axis=1, concat_axis=1, tiled=True)
    attended = attend(arrived_heads.reshape(3, seq_count, heads_here, HEAD_DIM, tok_rows))
    attended = attended.reshape(seq_count, tok_rows, 1, head_width)
    token_heads = lax.all_to_all(attended, "seq", split_axis=0, concat_axis=2, tiled=True).reshape(
        tok_rows, model_width
    )
    projected_sum = jnp.dot(
        token_heads,
        lax.all_gather(attn_proj, "seq", axis=0, tiled=True),
        preferred_element_type=jnp.float32,
    )
    stream_own = residual[0].astype(jnp.float32) + projected_sum
    stream = stream_own.astype(jnp.bfloat16)
    stream_own = stream.astype(jnp.float32)
    normed = layer_norm(stream, norm_gain, norm_bias)
    seq_index = lax.axis_index("seq")
    ids_own = lax.dynamic_slice_in_dim(expert_ids[0, :, 0], seq_index * tok_rows, tok_rows)
    onehot = (ids_own[:, None] == jnp.arange(experts, dtype=jnp.int32)[None, :]).astype(jnp.int32)
    before = jnp.cumsum(onehot, axis=0) - onehot
    order_in_block = jnp.sum(before * onehot, axis=1)
    dest = ids_own * cap_dev + order_in_block
    select = (dest[:, None] == jnp.arange(experts * cap_dev, dtype=jnp.int32)[None, :]).astype(
        jnp.bfloat16
    ).reshape(tok_rows, exp_count, local_experts, cap_dev)
    dispatch = jnp.einsum(
        "tgjc,td->gjcd", select, normed, preferred_element_type=jnp.float32
    ).astype(jnp.bfloat16)
    arrived = lax.all_to_all(dispatch, "exp", split_axis=0, concat_axis=0, tiled=True)
    gathered = lax.all_gather(arrived, "seq", axis=0, tiled=False)
    pieces = []
    for local in range(local_experts):
        hidden = jax.nn.gelu(
            jnp.einsum(
                "secd,df->secf",
                gathered[:, :, local],
                expert_up[local],
                preferred_element_type=jnp.float32,
            ),
            approximate=False,
        ).astype(jnp.bfloat16)
        hidden = lax.optimization_barrier(hidden)
        piece = jnp.einsum(
            "secf,fd->secd", hidden, expert_down[local], preferred_element_type=jnp.float32
        )
        pieces.append(piece.astype(jnp.bfloat16))
    pieces = jnp.stack(pieces, axis=2)
    summed = lax.psum_scatter(pieces, "seq", scatter_dimension=0, tiled=True)[0]
    returned = lax.all_to_all(summed, "exp", split_axis=0, concat_axis=0, tiled=True)
    expert_out = jnp.einsum(
        "tgjc,gjcd->td", select, returned, preferred_element_type=jnp.float32
    )
    return (stream_own + expert_out).astype(jnp.bfloat16)[None]


def solution(mesh):
    return jax.shard_map(
        per_device,
        mesh=mesh,
        in_specs=(
            P(("img", "exp"), "seq", None, None),
            P(("img", "exp"), "seq", None),
            P("seq", None),
            P(),
            P(),
            P(("img", "exp"), None, None),
            P("exp", None, "seq"),
            P("exp", "seq", None),
        ),
        out_specs=P(("img", "exp"), "seq", None),
        check_vma=False,
    )
```

```python
import jax
import jax.numpy as jnp
from jax import lax
from jax.sharding import PartitionSpec as P

HEADS = 16
HEAD_DIM = 80


def attend(gathered):
    queries = gathered[0]
    keys_all = gathered[1]
    values = gathered[2]
    factor = 1.0 / queries.shape[2] ** 0.5
    scores = (
        jnp.einsum("ahdb,chde->habce", queries, keys_all, preferred_element_type=jnp.float32)
        * factor
    )
    peak = jnp.max(scores, axis=(3, 4), keepdims=True)
    powers = jnp.exp(scores - peak)
    weights = (powers / jnp.sum(powers, axis=(3, 4), keepdims=True)).astype(jnp.bfloat16)
    mixed = jnp.einsum("habce,chde->abhd", weights, values, preferred_element_type=jnp.float32)
    return mixed.astype(jnp.bfloat16)


def layer_norm(stream, norm_gain, norm_bias):
    values = stream.astype(jnp.float32)
    centre = jnp.mean(values, axis=-1, keepdims=True)
    centered = values - centre
    variance = jnp.mean(centered * centered, axis=-1, keepdims=True)
    return (centered / jnp.sqrt(variance + 1e-06) * norm_gain + norm_bias).astype(jnp.bfloat16)


def per_device(
    projected, residual, attn_proj, norm_gain, norm_bias, expert_ids, expert_up, expert_down
):
    tok_rows = projected.shape[1]
    model_width = projected.shape[3]
    seq_count = lax.axis_size("seq")
    exp_count = lax.axis_size("exp")
    local_experts = expert_up.shape[0]
    experts = local_experts * exp_count
    cap_dev = 3 * tok_rows // (2 * experts)
    capacity = cap_dev * seq_count
    length = tok_rows * seq_count
    heads_here = HEADS // seq_count
    head_width = heads_here * HEAD_DIM
    token_minor = jnp.transpose(projected[0], (1, 2, 0)).reshape(
        3, seq_count, head_width, tok_rows
    )
    arrived_heads = lax.all_to_all(token_minor, "seq", split_axis=1, concat_axis=1, tiled=True)
    attended = attend(arrived_heads.reshape(3, seq_count, heads_here, HEAD_DIM, tok_rows))
    attended = attended.reshape(seq_count, tok_rows, 1, head_width)
    token_heads = lax.all_to_all(attended, "seq", split_axis=0, concat_axis=2, tiled=True).reshape(
        tok_rows, model_width
    )
    projected_sum = jnp.dot(
        token_heads,
        lax.all_gather(attn_proj, "seq", axis=0, tiled=True),
        preferred_element_type=jnp.float32,
    )
    stream_own = residual[0].astype(jnp.float32) + projected_sum
    stream = stream_own.astype(jnp.bfloat16)
    stream_own = stream.astype(jnp.float32)
    normed = layer_norm(stream, norm_gain, norm_bias)
    seq_index = lax.axis_index("seq")
    ids_own = lax.dynamic_slice_in_dim(expert_ids[0, :, 0], seq_index * tok_rows, tok_rows)
    onehot = (ids_own[:, None] == jnp.arange(experts, dtype=jnp.int32)[None, :]).astype(jnp.int32)
    before = jnp.cumsum(onehot, axis=0) - onehot
    order_in_block = jnp.sum(before * onehot, axis=1)
    dest = ids_own * cap_dev + order_in_block
    select = (dest[:, None] == jnp.arange(experts * cap_dev, dtype=jnp.int32)[None, :]).astype(
        jnp.bfloat16
    ).reshape(tok_rows, exp_count, local_experts, cap_dev)
    dispatch = jnp.einsum(
        "tgjc,td->gjcd", select, normed, preferred_element_type=jnp.float32
    ).astype(jnp.bfloat16)
    arrived = lax.all_to_all(dispatch, "exp", split_axis=0, concat_axis=0, tiled=True)
    gathered = lax.all_gather(arrived, "seq", axis=0, tiled=False)
    pieces = []
    for local in range(local_experts):
        lifted = jnp.einsum(
            "secd,df->secf",
            gathered[:, :, local],
            expert_up[local],
            preferred_element_type=jnp.float32,
        )
        hidden = (0.5 * lifted * (1.0 + lax.erf(lifted * (0.5**0.5)))).astype(jnp.bfloat16)
        hidden = lax.optimization_barrier(hidden)
        piece = jnp.einsum(
            "secf,fd->secd", hidden, expert_down[local], preferred_element_type=jnp.float32
        )
        pieces.append(piece.astype(jnp.bfloat16))
    pieces = jnp.stack(pieces, axis=2)
    summed = lax.psum_scatter(pieces, "seq", scatter_dimension=0, tiled=True)[0]
    returned = lax.all_to_all(summed, "exp", split_axis=0, concat_axis=0, tiled=True)
    expert_out = jnp.einsum(
        "tgjc,gjcd->td", select, returned, preferred_element_type=jnp.float32
    )
    return (stream_own + expert_out).astype(jnp.bfloat16)[None]


def solution(mesh):
    return jax.shard_map(
        per_device,
        mesh=mesh,
        in_specs=(
            P(("img", "exp"), "seq", None, None),
            P(("img", "exp"), "seq", None),
            P("seq", None),
            P(),
            P(),
            P(("img", "exp"), None, None),
            P("exp", None, "seq"),
            P("exp", "seq", None),
        ),
        out_specs=P(("img", "exp"), "seq", None),
        check_vma=False,
    )
```

```python
import jax
import jax.numpy as jnp
from jax import lax
from jax.sharding import PartitionSpec as P

HEADS = 16
HEAD_DIM = 80


def attend(gathered):
    queries = gathered[0]
    keys_all = gathered[1]
    values = gathered[2]
    factor = 1.0 / queries.shape[2] ** 0.5
    scores = (
        jnp.einsum("ahdb,chde->habce", queries, keys_all, preferred_element_type=jnp.float32)
        * factor
    )
    peak = jnp.max(scores, axis=(3, 4), keepdims=True)
    powers = jnp.exp(scores - peak)
    weights = (powers / jnp.sum(powers, axis=(3, 4), keepdims=True)).astype(jnp.bfloat16)
    mixed = jnp.einsum("habce,chde->abhd", weights, values, preferred_element_type=jnp.float32)
    return mixed.astype(jnp.bfloat16)


def layer_norm(stream, norm_gain, norm_bias):
    values = stream.astype(jnp.float32)
    centre = jnp.mean(values, axis=-1, keepdims=True)
    centered = values - centre
    variance = jnp.mean(centered * centered, axis=-1, keepdims=True)
    return (centered / jnp.sqrt(variance + 1e-06) * norm_gain + norm_bias).astype(jnp.bfloat16)


def per_device(
    projected, residual, attn_proj, norm_gain, norm_bias, expert_ids, expert_up, expert_down
):
    tok_rows = projected.shape[1]
    model_width = projected.shape[3]
    seq_count = lax.axis_size("seq")
    exp_count = lax.axis_size("exp")
    local_experts = expert_up.shape[0]
    experts = local_experts * exp_count
    cap_dev = 3 * tok_rows // (2 * experts)
    capacity = cap_dev * seq_count
    length = tok_rows * seq_count
    heads_here = HEADS // seq_count
    head_width = heads_here * HEAD_DIM
    token_minor = jnp.transpose(projected[0], (1, 2, 0)).reshape(
        3, seq_count, head_width, tok_rows
    )
    arrived_heads = lax.all_to_all(token_minor, "seq", split_axis=1, concat_axis=1, tiled=True)
    attended = attend(arrived_heads.reshape(3, seq_count, heads_here, HEAD_DIM, tok_rows))
    attended = attended.reshape(seq_count, tok_rows, 1, head_width)
    token_heads = lax.all_to_all(attended, "seq", split_axis=0, concat_axis=2, tiled=True).reshape(
        tok_rows, model_width
    )
    img_count = lax.axis_size("img")
    core = lax.axis_index("img") % 2
    half_width = model_width // 2
    proj_half = lax.all_gather(
        lax.dynamic_slice_in_dim(attn_proj, core * half_width, half_width, axis=1),
        "seq",
        axis=0,
        tiled=True,
    )
    proj_other = lax.ppermute(proj_half, "img", [(i, i ^ 1) for i in range(img_count)])
    sum_half = jnp.dot(token_heads, proj_half, preferred_element_type=jnp.float32)
    sum_other = jnp.dot(token_heads, proj_other, preferred_element_type=jnp.float32)
    projected_sum = jnp.where(
        core == 0,
        jnp.concatenate([sum_half, sum_other], axis=1),
        jnp.concatenate([sum_other, sum_half], axis=1),
    )
    stream_own = residual[0].astype(jnp.float32) + projected_sum
    stream = stream_own.astype(jnp.bfloat16)
    stream_own = stream.astype(jnp.float32)
    normed = layer_norm(stream, norm_gain, norm_bias)
    seq_index = lax.axis_index("seq")
    ids_own = lax.dynamic_slice_in_dim(expert_ids[0, :, 0], seq_index * tok_rows, tok_rows)
    onehot = (ids_own[:, None] == jnp.arange(experts, dtype=jnp.int32)[None, :]).astype(jnp.int32)
    before = jnp.cumsum(onehot, axis=0) - onehot
    order_in_block = jnp.sum(before * onehot, axis=1)
    dest = ids_own * cap_dev + order_in_block
    select = (dest[:, None] == jnp.arange(experts * cap_dev, dtype=jnp.int32)[None, :]).astype(
        jnp.bfloat16
    ).reshape(tok_rows, exp_count, local_experts, cap_dev)
    dispatch = jnp.einsum(
        "tgjc,td->gjcd", select, normed, preferred_element_type=jnp.float32
    ).astype(jnp.bfloat16)
    arrived = lax.all_to_all(dispatch, "exp", split_axis=0, concat_axis=0, tiled=True)
    gathered = lax.all_gather(arrived, "seq", axis=0, tiled=False)
    pieces = []
    for local in range(local_experts):
        lifted = jnp.einsum(
            "secd,df->secf",
            gathered[:, :, local],
            expert_up[local],
            preferred_element_type=jnp.float32,
        )
        hidden = (0.5 * lifted * (1.0 + lax.erf(lifted * (0.5**0.5)))).astype(jnp.bfloat16)
        hidden = lax.optimization_barrier(hidden)
        piece = jnp.einsum(
            "secf,fd->secd", hidden, expert_down[local], preferred_element_type=jnp.float32
        )
        pieces.append(piece.astype(jnp.bfloat16))
    pieces = jnp.stack(pieces, axis=2)
    summed = lax.psum_scatter(pieces, "seq", scatter_dimension=0, tiled=True)[0]
    returned = lax.all_to_all(summed, "exp", split_axis=0, concat_axis=0, tiled=True)
    expert_out = jnp.einsum(
        "tgjc,gjcd->td", select, returned, preferred_element_type=jnp.float32
    )
    return (stream_own + expert_out).astype(jnp.bfloat16)[None]


def solution(mesh):
    return jax.shard_map(
        per_device,
        mesh=mesh,
        in_specs=(
            P(("img", "exp"), "seq", None, None),
            P(("img", "exp"), "seq", None),
            P("seq", None),
            P(),
            P(),
            P(("img", "exp"), None, None),
            P("exp", None, "seq"),
            P("exp", "seq", None),
        ),
        out_specs=P(("img", "exp"), "seq", None),
        check_vma=False,
    )
```

```python
import jax
import jax.numpy as jnp
from jax import lax
from jax.sharding import PartitionSpec as P

HEADS = 16
HEAD_DIM = 80


def attend(gathered):
    queries = gathered[0]
    keys_all = gathered[1]
    values = gathered[2]
    factor = 1.0 / queries.shape[2] ** 0.5
    scores = (
        jnp.einsum("ahdb,chde->habce", queries, keys_all, preferred_element_type=jnp.float32)
        * factor
    )
    peak = jnp.max(scores, axis=(3, 4), keepdims=True)
    powers = jnp.exp(scores - peak)
    weights = (powers * (1.0 / jnp.sum(powers, axis=(3, 4), keepdims=True))).astype(jnp.bfloat16)
    mixed = jnp.einsum("habce,chde->abhd", weights, values, preferred_element_type=jnp.float32)
    return mixed.astype(jnp.bfloat16)


def layer_norm(stream, norm_gain, norm_bias):
    values = stream.astype(jnp.float32)
    centre = jnp.mean(values, axis=-1, keepdims=True)
    centered = values - centre
    variance = jnp.mean(centered * centered, axis=-1, keepdims=True)
    return (centered * lax.rsqrt(variance + 1e-06) * norm_gain + norm_bias).astype(jnp.bfloat16)


def per_device(
    projected, residual, attn_proj, norm_gain, norm_bias, expert_ids, expert_up, expert_down
):
    tok_rows = projected.shape[1]
    model_width = projected.shape[3]
    seq_count = lax.axis_size("seq")
    exp_count = lax.axis_size("exp")
    local_experts = expert_up.shape[0]
    experts = local_experts * exp_count
    cap_dev = 3 * tok_rows // (2 * experts)
    capacity = cap_dev * seq_count
    length = tok_rows * seq_count
    heads_here = HEADS // seq_count
    head_width = heads_here * HEAD_DIM
    token_minor = jnp.transpose(projected[0], (1, 2, 0)).reshape(
        3, seq_count, head_width, tok_rows
    )
    arrived_heads = lax.all_to_all(token_minor, "seq", split_axis=1, concat_axis=1, tiled=True)
    attended = attend(arrived_heads.reshape(3, seq_count, heads_here, HEAD_DIM, tok_rows))
    attended = attended.reshape(seq_count, tok_rows, 1, head_width)
    token_heads = lax.all_to_all(attended, "seq", split_axis=0, concat_axis=2, tiled=True).reshape(
        tok_rows, model_width
    )
    projected_sum = jnp.dot(
        token_heads,
        lax.all_gather(attn_proj, "seq", axis=0, tiled=True),
        preferred_element_type=jnp.float32,
    )
    stream_own = residual[0].astype(jnp.float32) + projected_sum
    stream = stream_own.astype(jnp.bfloat16)
    stream_own = stream.astype(jnp.float32)
    normed = layer_norm(stream, norm_gain, norm_bias)
    seq_index = lax.axis_index("seq")
    ids_own = lax.dynamic_slice_in_dim(expert_ids[0, :, 0], seq_index * tok_rows, tok_rows)
    onehot = (ids_own[:, None] == jnp.arange(experts, dtype=jnp.int32)[None, :]).astype(jnp.int32)
    before = jnp.cumsum(onehot, axis=0) - onehot
    order_in_block = jnp.sum(before * onehot, axis=1)
    dest = ids_own * cap_dev + order_in_block
    select = (dest[:, None] == jnp.arange(experts * cap_dev, dtype=jnp.int32)[None, :]).astype(
        jnp.bfloat16
    ).reshape(tok_rows, exp_count, local_experts, cap_dev)
    dispatch = jnp.einsum(
        "tgjc,td->gjcd", select, normed, preferred_element_type=jnp.float32
    ).astype(jnp.bfloat16)
    arrived = lax.all_to_all(dispatch, "exp", split_axis=0, concat_axis=0, tiled=True)
    gathered = lax.all_gather(arrived, "seq", axis=0, tiled=False)
    pieces = []
    for local in range(local_experts):
        lifted = jnp.einsum(
            "secd,df->secf",
            gathered[:, :, local],
            expert_up[local],
            preferred_element_type=jnp.float32,
        )
        hidden = (0.5 * lifted * (1.0 + lax.erf(lifted * (0.5**0.5)))).astype(jnp.bfloat16)
        hidden = lax.optimization_barrier(hidden)
        piece = jnp.einsum(
            "secf,fd->secd", hidden, expert_down[local], preferred_element_type=jnp.float32
        )
        pieces.append(piece.astype(jnp.bfloat16))
    pieces = jnp.stack(pieces, axis=2)
    summed = lax.psum_scatter(pieces, "seq", scatter_dimension=0, tiled=True)[0]
    returned = lax.all_to_all(summed, "exp", split_axis=0, concat_axis=0, tiled=True)
    expert_out = jnp.einsum(
        "tgjc,gjcd->td", select, returned, preferred_element_type=jnp.float32
    )
    return (stream_own + expert_out).astype(jnp.bfloat16)[None]


def solution(mesh):
    return jax.shard_map(
        per_device,
        mesh=mesh,
        in_specs=(
            P(("img", "exp"), "seq", None, None),
            P(("img", "exp"), "seq", None),
            P("seq", None),
            P(),
            P(),
            P(("img", "exp"), None, None),
            P("exp", None, "seq"),
            P("exp", "seq", None),
        ),
        out_specs=P(("img", "exp"), "seq", None),
        check_vma=False,
    )
```

```python
import jax
import jax.numpy as jnp
from jax import lax
from jax.sharding import PartitionSpec as P

HEADS = 16
HEAD_DIM = 80


def attend(gathered):
    queries = gathered[0]
    keys_all = gathered[1]
    values = gathered[2]
    factor = 1.0 / queries.shape[2] ** 0.5
    scores = (
        jnp.einsum("ahdb,chde->habce", queries, keys_all, preferred_element_type=jnp.float32)
        * factor
    )
    peak = jnp.max(scores, axis=(3, 4), keepdims=True)
    powers = jnp.exp(scores - peak)
    weights = (powers * (1.0 / jnp.sum(powers, axis=(3, 4), keepdims=True))).astype(jnp.bfloat16)
    mixed = jnp.einsum("habce,chde->abhd", weights, values, preferred_element_type=jnp.float32)
    return mixed.astype(jnp.bfloat16)


def layer_norm(stream, norm_gain, norm_bias):
    values = stream.astype(jnp.float32)
    centre = jnp.mean(values, axis=-1, keepdims=True)
    centered = values - centre
    variance = jnp.mean(centered * centered, axis=-1, keepdims=True)
    return (centered * lax.rsqrt(variance + 1e-06) * norm_gain + norm_bias).astype(jnp.bfloat16)


def per_device(
    projected, residual, attn_proj, norm_gain, norm_bias, expert_ids, expert_up, expert_down
):
    tok_rows = projected.shape[1]
    model_width = projected.shape[3]
    seq_count = lax.axis_size("seq")
    exp_count = lax.axis_size("exp")
    local_experts = expert_up.shape[0]
    experts = local_experts * exp_count
    cap_dev = 3 * tok_rows // (2 * experts)
    capacity = cap_dev * seq_count
    length = tok_rows * seq_count
    heads_here = HEADS // seq_count
    head_width = heads_here * HEAD_DIM
    token_minor = jnp.transpose(projected[0], (1, 2, 0)).reshape(
        3, seq_count, head_width, tok_rows
    )
    arrived_heads = lax.all_to_all(token_minor, "seq", split_axis=1, concat_axis=1, tiled=True)
    attended = attend(arrived_heads.reshape(3, seq_count, heads_here, HEAD_DIM, tok_rows))
    attended = attended.reshape(seq_count, tok_rows, 1, head_width)
    token_heads = lax.all_to_all(attended, "seq", split_axis=0, concat_axis=2, tiled=True).reshape(
        tok_rows, model_width
    )
    projected_sum = jnp.dot(
        token_heads,
        lax.all_gather(attn_proj, "seq", axis=0, tiled=True),
        preferred_element_type=jnp.float32,
    )
    stream_own = residual[0].astype(jnp.float32) + projected_sum
    stream = stream_own.astype(jnp.bfloat16)
    stream_own = stream.astype(jnp.float32)
    normed = layer_norm(stream, norm_gain, norm_bias)
    seq_index = lax.axis_index("seq")
    ids_own = lax.dynamic_slice_in_dim(expert_ids[0, :, 0], seq_index * tok_rows, tok_rows)
    onehot = (ids_own[:, None] == jnp.arange(experts, dtype=jnp.int32)[None, :]).astype(jnp.int32)
    before = jnp.cumsum(onehot, axis=0) - onehot
    order_in_block = jnp.sum(before * onehot, axis=1)
    dest = ids_own * cap_dev + order_in_block
    select = (dest[:, None] == jnp.arange(experts * cap_dev, dtype=jnp.int32)[None, :]).astype(
        jnp.bfloat16
    ).reshape(tok_rows, exp_count, local_experts, cap_dev)
    dispatch = jnp.einsum(
        "tgjc,td->gjcd", select, normed, preferred_element_type=jnp.float32
    ).astype(jnp.bfloat16)
    arrived = lax.all_to_all(dispatch, "exp", split_axis=0, concat_axis=0, tiled=True)
    gathered = lax.all_gather(arrived, "seq", axis=0, tiled=False)
    hid_local = expert_up.shape[2]
    rows = gathered.reshape(-1, model_width)
    up_both = jnp.transpose(expert_up, (1, 0, 2)).reshape(model_width, local_experts * hid_local)
    lifted = jnp.dot(rows, up_both, preferred_element_type=jnp.float32)
    row_expert = (jnp.arange(rows.shape[0], dtype=jnp.int32) // cap_dev) % local_experts
    col_expert = jnp.arange(local_experts * hid_local, dtype=jnp.int32) // hid_local
    own = row_expert[:, None] == col_expert[None, :]
    activated = 0.5 * lifted * (1.0 + lax.erf(lifted * (0.5**0.5)))
    hidden = lax.optimization_barrier(jnp.where(own, activated, 0.0).astype(jnp.bfloat16))
    down_both = expert_down.reshape(local_experts * hid_local, model_width)
    pieces = jnp.dot(hidden, down_both, preferred_element_type=jnp.float32).astype(jnp.bfloat16)
    pieces = pieces.reshape(gathered.shape)
    summed = lax.psum_scatter(pieces, "seq", scatter_dimension=0, tiled=True)[0]
    returned = lax.all_to_all(summed, "exp", split_axis=0, concat_axis=0, tiled=True)
    expert_out = jnp.einsum(
        "tgjc,gjcd->td", select, returned, preferred_element_type=jnp.float32
    )
    return (stream_own + expert_out).astype(jnp.bfloat16)[None]


def solution(mesh):
    return jax.shard_map(
        per_device,
        mesh=mesh,
        in_specs=(
            P(("img", "exp"), "seq", None, None),
            P(("img", "exp"), "seq", None),
            P("seq", None),
            P(),
            P(),
            P(("img", "exp"), None, None),
            P("exp", None, "seq"),
            P("exp", "seq", None),
        ),
        out_specs=P(("img", "exp"), "seq", None),
        check_vma=False,
    )
```
